256 devices in a mesh: sensor: 8 (over z_lo, core), tm: 32 (over x, y, z_hi).
Axes of the slice: x: 4, y: 4, z: 8 (z_hi: 2, z_lo: 4; z = z_hi * 4 + z_lo), core: 2. Of those that a mesh axis runs over, the one named last changes fastest.
Arguments:
- readings: float32 [4096, 128], P(('sensor', 'tm')), may hold values from -18 to 18
- noise_var: float32 [4096, 128], P(('sensor', 'tm')), may hold values from 0.1 to 1
- sensor_weights: float32 [4096, 64, 128], P(('sensor', 'tm')), may hold values from -0.1 to 1, as said below
- time_weights: float32 [4096, 128, 128], P(('sensor', 'tm')), may hold values from -0.1 to 1, as said below
- window_index: int32 [4096], P(('sensor', 'tm')), may hold values from 0 to 7
- sensor_kernel: float32 [4096, 4096], P('sensor'), may hold values from -1 to 1.5, as said below
- time_kernel: float32 [4096, 4096], P('tm'), may hold values from -1 to 1.5, as said below
Outputs:
- solution: float32 [4096, 128], P(('sensor', 'tm'))
- residual: float32 [4096, 128], P(('sensor', 'tm'))
The draws below stay inside these ranges and needn't reach their ends.
Inputs may be any that keep to these rules, and one draw needn't show every extreme that they name: Block b's readings interpolate from sensor rows 64 * window_index[b] to 64 * window_index[b] + 63 of the sensor rows that its device holds. `sensor_weights`: each reading's column holds the four cubic convolution weights of one position, in rows p - 1 to p + 2 for some p with 1 <= p <= 61; the other entries are zero. `time_weights`: each reading's column holds the four cubic convolution weights of one position, in rows p - 1 to p + 2 for some p with 1 <= p <= 125; the other entries are zero. `sensor_kernel`: symmetric and positive definite. `time_kernel`: symmetric and positive definite.
All inputs are finite; a program needn't handle non-finite values.
Results may differ from the reference program's by a relative error of at most 0.0003.
Values sent between devices are 32-bit elements; how exact they have to be, the bound alone decides.
No kernel may reach another device: no remote copies, remote signals or barrier semaphores. Data moves between devices by JAX's collectives and lax.ppermute only.
A program may use at most 64 MiB of HBM per device.

```python
import math
import jax
import jax.numpy as jnp
from jax import lax

SENSORS = 4096
TIMES = 4096
SWIN = 64
RB = 128
BLK_DEV = 16
ITERS = 2
TIME_DEV = 128
WINS = 8
BLOCKS = 4096
N_SENSOR = 8
N_TM = 32


def cubic_tile(key, window_len):
    key_anchor, key_fraction = jax.random.split(key)
    anchor = jax.random.randint(key_anchor, (BLOCKS, RB), 1, window_len - 2)
    fraction = jax.random.uniform(key_fraction, (BLOCKS, RB), jnp.float32)
    cube = fraction * fraction * fraction
    square = fraction * fraction
    stencil = (-0.5 * cube + square - 0.5 * fraction, 1.5 * cube - 2.5 * square + 1.0, -1.5 * cube + 2.0 * square + 0.5 * fraction, 0.5 * cube - 0.5 * square)
    positions = jnp.arange(window_len, dtype=jnp.int32)[None, :, None]
    first_row = (anchor - 1)[:, None, :]
    dense_tile = jnp.zeros((BLOCKS, window_len, RB), jnp.float32)
    for offset in range(4):
        dense_tile = dense_tile + jnp.where(positions == first_row + offset, stencil[offset][:, None, :], 0.0)
    return dense_tile


def symmetric_kernel(key, matrix_order):
    key_entries, key_diagonal = jax.random.split(key)
    spread = 0.735
    matrix = jax.random.uniform(key_entries, (matrix_order, matrix_order), jnp.float32, -1.0, 1.0)
    symmetric = (matrix + matrix.T) * (0.5 * spread / math.sqrt(matrix_order))
    diagonal = 1.0 + 0.5 * jax.random.uniform(key_diagonal, (matrix_order,), jnp.float32)
    identity = jnp.eye(matrix_order, dtype=jnp.float32)
    return symmetric * (1.0 - identity) + identity * diagonal[None, :]


def draw_readings(key, part):
    position = jnp.arange(BLOCKS, dtype=jnp.float32)[:, None] / max(BLOCKS - 1, 1)
    raw_values = jnp.clip(jax.random.normal(key, (BLOCKS, RB), jnp.float32), -6.0, 6.0)
    return raw_values * (1.0 + 2.0 * position)


def draw_sensor_weights(key, part):
    return cubic_tile(jax.random.fold_in(key, 11), SWIN)


def draw_time_weights(key, part):
    return cubic_tile(jax.random.fold_in(key, 23), TIME_DEV)


def draw_sensor_kernel(key, part):
    return symmetric_kernel(jax.random.fold_in(key, 31), SENSORS)


def draw_time_kernel(key, part):
    return symmetric_kernel(jax.random.fold_in(key, 47), TIMES)


def plant(array, own_key, least, largest):
    longest = array.shape.index(max(array.shape))
    spots = []
    for shift in (0, 1):
        where = [jax.random.randint(jax.random.fold_in(own_key, axis), (), 0, length) for axis, length in enumerate(array.shape)]
        where[longest] = (where[longest] + shift) % array.shape[longest]
        spots.append(tuple(where))
    return array.at[spots[0]].set(least).at[spots[1]].set(largest)


def levels(stream_key, extent, pieces, low, top_value):
    def one(dim, shards_of):
        heights = jax.random.uniform(jax.random.fold_in(jax.random.fold_in(stream_key, 6), dim), (shards_of,), jnp.float32, low / len(pieces), top_value / len(pieces))
        return jnp.repeat(jnp.exp(heights), extent[dim] // shards_of).reshape((-1,) + (1,) * (len(extent) - dim - 1))

    factor_of = one(*pieces[0])
    for cut in pieces[1:]:
        factor_of = factor_of * one(*cut)
    return factor_of


def setup_inputs(seed: int = 0) -> dict:
    splits = jax.random.split(jax.random.key(seed), 8)
    return {
        "readings": draw_readings(jax.random.fold_in(splits[7], 71), 0),
        "noise_var": jnp.clip(jnp.exp(math.log(1.0) - 2.3025851 * jax.random.uniform(splits[1], (BLOCKS, RB), jnp.float32) ** levels(splits[1], (BLOCKS, RB), ((0, 256),), -0.2, 0.2)), 0.1, 1.0),
        "sensor_weights": draw_sensor_weights(jax.random.fold_in(splits[7], 71), 0),
        "time_weights": draw_time_weights(jax.random.fold_in(splits[7], 71), 0),
        "window_index": plant(jax.random.randint(splits[4], (BLOCKS,), 0, WINS), jax.random.fold_in(splits[4], 1), 0, WINS - 1).astype(jnp.int32),
        "sensor_kernel": draw_sensor_kernel(jax.random.fold_in(splits[7], 71), 0),
        "time_kernel": draw_time_kernel(jax.random.fold_in(splits[7], 71), 0),
    }


PRECISE = lax.Precision.HIGHEST


def reference(readings, noise_var, sensor_weights, time_weights, window_index, sensor_kernel, time_kernel):
    lead = (N_SENSOR, N_TM, BLK_DEV)
    onehot = (window_index.reshape(lead)[..., None] == jnp.arange(WINS, dtype=jnp.int32)).astype(jnp.float32)
    sensor_tile = sensor_weights.reshape(lead + (SWIN, RB))
    time_tile = time_weights.reshape(lead + (TIME_DEV, RB))
    noise_blocks = noise_var.reshape(lead + (RB,))

    kernel_grid = sensor_kernel.reshape(N_SENSOR, WINS, SWIN, N_SENSOR, WINS, SWIN)
    sensor_ids = jnp.arange(N_SENSOR, dtype=jnp.int32)[:, None]
    window_ids = jnp.arange(WINS, dtype=jnp.int32)[None, :]
    window_kernel = kernel_grid[sensor_ids, window_ids, :, sensor_ids, window_ids, :]
    block_kernel = jnp.einsum('stbw,swik->stbik', onehot, window_kernel, precision=PRECISE)
    sensor_quad = jnp.sum(sensor_tile * jnp.einsum('stbik,stbkr->stbir', block_kernel, sensor_tile, precision=PRECISE), axis=3)
    time_grid = time_kernel.reshape(N_TM, TIME_DEV, N_TM, TIME_DEV)
    time_ids = jnp.arange(N_TM, dtype=jnp.int32)
    time_square = time_grid[time_ids, :, time_ids, :]
    time_quad = jnp.sum(time_tile * jnp.einsum('tjl,stblr->stbjr', time_square, time_tile, precision=PRECISE), axis=3)
    inverse = 1.0 / (sensor_quad * time_quad + noise_blocks)

    def operator_apply(vector):
        scaled = vector[:, :, :, None, :] * time_tile
        contrib = jnp.einsum('stbir,stbjr->stbij', sensor_tile, scaled, precision=PRECISE)
        grid_field = jnp.einsum('stbw,stbij->switj', onehot, contrib, precision=PRECISE).reshape(SENSORS, TIMES)
        left_product = jnp.dot(sensor_kernel, grid_field, precision=PRECISE, preferred_element_type=jnp.float32)
        smooth = jnp.dot(left_product, time_kernel.T, precision=PRECISE, preferred_element_type=jnp.float32)
        smooth = smooth.reshape(N_SENSOR, WINS, SWIN, N_TM, TIME_DEV)
        gathered = jnp.einsum('stbw,switj->stbij', onehot, smooth, precision=PRECISE)
        interp_cols = jnp.einsum('stbij,stbjr->stbir', gathered, time_tile, precision=PRECISE)
        return jnp.sum(sensor_tile * interp_cols, axis=3) + noise_blocks * vector

    residual = readings.reshape(lead + (RB,))
    solution = jnp.zeros_like(residual)
    precond = inverse * residual
    direction = precond
    inner_now = jnp.sum(residual * precond)
    for iteration in range(ITERS):
        image_vec = operator_apply(direction)
        step_size = inner_now / jnp.sum(direction * image_vec)
        solution = solution + step_size * direction
        residual = residual - step_size * image_vec
        if iteration + 1 < ITERS:
            precond = inverse * residual
            inner_next = jnp.sum(residual * precond)
            direction = precond + (inner_next / inner_now) * direction
            inner_now = inner_next
    return solution.reshape(BLOCKS, RB), residual.reshape(BLOCKS, RB)
```

```python
import jax
import jax.numpy as jnp
from jax import lax
from jax.sharding import PartitionSpec as P

PRECISE = lax.Precision.HIGHEST
PAY_ROWS = 8


def on_device(
    readings, noise_var, sensor_weights, time_weights, window_index, sensor_kernel, time_kernel
):
    sensor_dev = sensor_kernel.shape[0]
    time_dev = time_kernel.shape[0]
    win_rows = sensor_weights.shape[1]
    win_count = sensor_dev // win_rows
    n_tm = time_kernel.shape[1] // time_dev
    window_ids = jnp.arange(win_count, dtype=jnp.int32)
    onehot = (window_index[:, None] == window_ids[None, :]).astype(jnp.float32)
    own_square = lax.dynamic_slice_in_dim(
        sensor_kernel, lax.axis_index("sensor") * sensor_dev, sensor_dev, 1
    )
    own_square = own_square.reshape(win_count, win_rows, win_count, win_rows)
    window_kernel = own_square[window_ids, :, window_ids, :]
    block_kernel = jnp.einsum("bw,wik->bik", onehot, window_kernel, precision=PRECISE)
    sensor_quad = jnp.sum(
        sensor_weights
        * jnp.einsum("bik,bkr->bir", block_kernel, sensor_weights, precision=PRECISE),
        axis=1,
    )
    time_square = lax.dynamic_slice_in_dim(
        time_kernel, lax.axis_index("tm") * time_dev, time_dev, 1
    )
    time_quad = jnp.sum(
        time_weights * jnp.einsum("jl,blr->bjr", time_square, time_weights, precision=PRECISE),
        axis=1,
    )
    inverse = 1.0 / (sensor_quad * time_quad + noise_var)

    def operator_apply(vector, payload=None):
        scaled = vector[:, None, :] * time_weights
        contrib = jnp.einsum("bir,bjr->bij", sensor_weights, scaled, precision=PRECISE)
        grid_field = jnp.einsum("bw,bij->wij", onehot, contrib, precision=PRECISE).reshape(
            sensor_dev, time_dev
        )
        if payload is None:
            full_field = lax.all_gather(grid_field, "sensor", axis=0, tiled=True)
        else:
            pad = jnp.zeros((PAY_ROWS, time_dev), jnp.float32)
            pad = pad.at[0, : payload.shape[0]].set(payload)
            both = lax.all_gather(
                jnp.concatenate([grid_field, pad], axis=0), "sensor", axis=0, tiled=False
            )
            full_field = both[:, :sensor_dev, :].reshape(-1, time_dev)
            sensor_sum = jnp.sum(both[:, sensor_dev:, :], axis=0)
        left_product = jnp.dot(
            sensor_kernel, full_field, precision=PRECISE, preferred_element_type=jnp.float32
        )
        if payload is not None:
            left_product = jnp.concatenate([left_product, sensor_sum], axis=0)
        gathered = lax.all_gather(left_product, "tm", axis=1, tiled=True)
        smooth = lax.dot_general(
            gathered[:sensor_dev],
            time_kernel,
            (((1,), (1,)), ((), ())),
            precision=PRECISE,
            preferred_element_type=jnp.float32,
        )
        field_rows = jnp.einsum(
            "bw,wij->bij", onehot, smooth.reshape(win_count, win_rows, time_dev), precision=PRECISE
        )
        interp_cols = jnp.einsum("bij,bjr->bir", field_rows, time_weights, precision=PRECISE)
        image = jnp.sum(sensor_weights * interp_cols, axis=1) + noise_var * vector
        if payload is None:
            return image, None
        totals = jnp.sum(
            gathered[sensor_dev:].reshape(PAY_ROWS, n_tm, time_dev), axis=1
        )[0, : payload.shape[0]]
        return image, totals

    residual0 = readings
    precond0 = inverse * residual0
    direction0 = precond0
    image0, _ = operator_apply(direction0)
    scaled_image0 = inverse * image0
    first_partials = jnp.stack(
        [jnp.sum(residual0 * precond0), jnp.sum(direction0 * image0)]
    )
    image_scaled, first_totals = operator_apply(scaled_image0, first_partials)
    inner0 = first_totals[0]
    step0 = inner0 / first_totals[1]
    solution = step0 * direction0
    residual1 = residual0 - step0 * image0
    precond1 = inverse * residual1
    image_precond1 = image0 - step0 * image_scaled
    second = lax.psum(
        jnp.stack(
            [
                jnp.sum(residual1 * precond1),
                jnp.sum(precond1 * image_precond1),
                jnp.sum(precond1 * image0 + direction0 * image_precond1),
            ]
        ),
        ("sensor", "tm"),
    )
    inner1 = second[0]
    ratio = inner1 / inner0
    direction1 = precond1 + ratio * direction0
    image1 = image_precond1 + ratio * image0
    curvature1 = second[1] + ratio * second[2] + ratio * ratio * first_totals[1]
    step1 = inner1 / curvature1
    solution = solution + step1 * direction1
    residual = residual1 - step1 * image1
    return (solution, residual)


def solution(mesh):
    in_specs = (
        P(("sensor", "tm"), None),
        P(("sensor", "tm"), None),
        P(("sensor", "tm"), None, None),
        P(("sensor", "tm"), None, None),
        P(("sensor", "tm")),
        P("sensor", None),
        P("tm", None),
    )
    out_specs = (P(("sensor", "tm"), None), P(("sensor", "tm"), None))
    return jax.shard_map(
        on_device, mesh=mesh, in_specs=in_specs, out_specs=out_specs, check_vma=False
    )
```

```python
import jax
import jax.numpy as jnp
from jax import lax
import numpy as np
from jax.sharding import Mesh, PartitionSpec as P

PRECISE = lax.Precision.HIGHEST
PAY_ROWS = 8
TM = ("tx", "ty", "tz")
ALL = ("sensor",) + TM


def tm_index():
    return (
        lax.axis_index("tx") * (lax.axis_size("ty") * lax.axis_size("tz"))
        + lax.axis_index("ty") * lax.axis_size("tz")
        + lax.axis_index("tz")
    )


def on_device(
    readings, noise_var, sensor_weights, time_weights, window_index, sensor_kernel, time_kernel
):
    sensor_dev = sensor_kernel.shape[0]
    time_dev = time_kernel.shape[0]
    win_rows = sensor_weights.shape[1]
    win_count = sensor_dev // win_rows
    n_tm = time_kernel.shape[1] // time_dev
    window_ids = jnp.arange(win_count, dtype=jnp.int32)
    onehot = (window_index[:, None] == window_ids[None, :]).astype(jnp.float32)
    own_square = lax.dynamic_slice_in_dim(
        sensor_kernel, lax.axis_index("sensor") * sensor_dev, sensor_dev, 1
    )
    own_square = own_square.reshape(win_count, win_rows, win_count, win_rows)
    window_kernel = own_square[window_ids, :, window_ids, :]
    block_kernel = jnp.einsum("bw,wik->bik", onehot, window_kernel, precision=PRECISE)
    sensor_quad = jnp.sum(
        sensor_weights
        * jnp.einsum("bik,bkr->bir", block_kernel, sensor_weights, precision=PRECISE),
        axis=1,
    )
    time_square = lax.dynamic_slice_in_dim(
        time_kernel, tm_index() * time_dev, time_dev, 1
    )
    time_quad = jnp.sum(
        time_weights * jnp.einsum("jl,blr->bjr", time_square, time_weights, precision=PRECISE),
        axis=1,
    )
    inverse = 1.0 / (sensor_quad * time_quad + noise_var)

    def operator_apply(vector, payload=None):
        scaled = vector[:, None, :] * time_weights
        contrib = jnp.einsum("bir,bjr->bij", sensor_weights, scaled, precision=PRECISE)
        grid_field = jnp.einsum("bw,bij->wij", onehot, contrib, precision=PRECISE).reshape(
            sensor_dev, time_dev
        )
        if payload is None:
            full_field = lax.all_gather(grid_field, "sensor", axis=0, tiled=True)
        else:
            pad = jnp.zeros((PAY_ROWS, time_dev), jnp.float32)
            pad = pad.at[0, : payload.shape[0]].set(payload)
            both = lax.all_gather(
                jnp.concatenate([grid_field, pad], axis=0), "sensor", axis=0, tiled=False
            )
            full_field = both[:, :sensor_dev, :].reshape(-1, time_dev)
            sensor_sum = jnp.sum(both[:, sensor_dev:, :], axis=0)
        left_product = jnp.dot(
            sensor_kernel, full_field, precision=PRECISE, preferred_element_type=jnp.float32
        )
        if payload is not None:
            left_product = jnp.concatenate([left_product, sensor_sum], axis=0)
        gathered = lax.all_gather(left_product, "tz", axis=1, tiled=True)
        gathered = lax.all_gather(gathered, ("tx", "ty"), axis=1, tiled=True)
        smooth = lax.dot_general(
            gathered[:sensor_dev],
            time_kernel,
            (((1,), (1,)), ((), ())),
            precision=PRECISE,
            preferred_element_type=jnp.float32,
        )
        field_rows = jnp.einsum(
            "bw,wij->bij", onehot, smooth.reshape(win_count, win_rows, time_dev), precision=PRECISE
        )
        interp_cols = jnp.einsum("bij,bjr->bir", field_rows, time_weights, precision=PRECISE)
        image = jnp.sum(sensor_weights * interp_cols, axis=1) + noise_var * vector
        if payload is None:
            return image, None
        totals = jnp.sum(
            gathered[sensor_dev:].reshape(PAY_ROWS, n_tm, time_dev), axis=1
        )[0, : payload.shape[0]]
        return image, totals

    residual0 = readings
    precond0 = inverse * residual0
    direction0 = precond0
    image0, _ = operator_apply(direction0)
    scaled_image0 = inverse * image0
    first_partials = jnp.stack(
        [jnp.sum(residual0 * precond0), jnp.sum(direction0 * image0)]
    )
    image_scaled, first_totals = operator_apply(scaled_image0, first_partials)
    inner0 = first_totals[0]
    step0 = inner0 / first_totals[1]
    solution = step0 * direction0
    residual1 = residual0 - step0 * image0
    precond1 = inverse * residual1
    image_precond1 = image0 - step0 * image_scaled
    second = lax.psum(
        jnp.stack(
            [
                jnp.sum(residual1 * precond1),
                jnp.sum(precond1 * image_precond1),
                jnp.sum(precond1 * image0 + direction0 * image_precond1),
            ]
        ),
        ALL,
    )
    inner1 = second[0]
    ratio = inner1 / inner0
    direction1 = precond1 + ratio * direction0
    image1 = image_precond1 + ratio * image0
    curvature1 = second[1] + ratio * second[2] + ratio * ratio * first_totals[1]
    step1 = inner1 / curvature1
    solution = solution + step1 * direction1
    residual = residual1 - step1 * image1
    return (solution, residual)


def solution(mesh):
    n_sensor, n_tm = mesh.devices.shape
    devices = np.asarray(mesh.devices).reshape(n_sensor, n_tm // 8, 4, 2)
    mesh = Mesh(devices, ("sensor",) + TM)
    in_specs = (
        P(ALL, None),
        P(ALL, None),
        P(ALL, None, None),
        P(ALL, None, None),
        P(ALL),
        P("sensor", None),
        P(TM, None),
    )
    out_specs = (P(ALL, None), P(ALL, None))
    return jax.shard_map(
        on_device, mesh=mesh, in_specs=in_specs, out_specs=out_specs, check_vma=False
    )
```

```python
import jax
import jax.numpy as jnp
from jax import lax
import numpy as np
from jax.sharding import Mesh, PartitionSpec as P

PRECISE = lax.Precision.HIGHEST
PAY_ROWS = 8
TM = ("tx", "ty", "tz")
ALL = ("sensor",) + TM


def tm_index():
    return (
        lax.axis_index("tx") * (lax.axis_size("ty") * lax.axis_size("tz"))
        + lax.axis_index("ty") * lax.axis_size("tz")
        + lax.axis_index("tz")
    )


def butterfly_sum(value):
    for axis in ALL:
        size = lax.axis_size(axis)
        stride = 1
        while stride < size:
            value = value + lax.ppermute(value, axis, [(i, i ^ stride) for i in range(size)])
            stride *= 2
    return value


def on_device(
    readings, noise_var, sensor_weights, time_weights, window_index, sensor_kernel, time_kernel
):
    sensor_dev = sensor_kernel.shape[0]
    time_dev = time_kernel.shape[0]
    win_rows = sensor_weights.shape[1]
    win_count = sensor_dev // win_rows
    n_tm = time_kernel.shape[1] // time_dev
    window_ids = jnp.arange(win_count, dtype=jnp.int32)
    onehot = (window_index[:, None] == window_ids[None, :]).astype(jnp.float32)
    own_square = lax.dynamic_slice_in_dim(
        sensor_kernel, lax.axis_index("sensor") * sensor_dev, sensor_dev, 1
    )
    own_square = own_square.reshape(win_count, win_rows, win_count, win_rows)
    window_kernel = own_square[window_ids, :, window_ids, :]
    block_kernel = jnp.einsum("bw,wik->bik", onehot, window_kernel, precision=PRECISE)
    sensor_quad = jnp.sum(
        sensor_weights
        * jnp.einsum("bik,bkr->bir", block_kernel, sensor_weights, precision=PRECISE),
        axis=1,
    )
    time_square = lax.dynamic_slice_in_dim(
        time_kernel, tm_index() * time_dev, time_dev, 1
    )
    time_quad = jnp.sum(
        time_weights * jnp.einsum("jl,blr->bjr", time_square, time_weights, precision=PRECISE),
        axis=1,
    )
    inverse = 1.0 / (sensor_quad * time_quad + noise_var)

    def operator_apply(vector, payload=None):
        scaled = vector[:, None, :] * time_weights
        contrib = jnp.einsum("bir,bjr->bij", sensor_weights, scaled, precision=PRECISE)
        grid_field = jnp.einsum("bw,bij->wij", onehot, contrib, precision=PRECISE).reshape(
            sensor_dev, time_dev
        )
        if payload is None:
            full_field = lax.all_gather(grid_field, "sensor", axis=0, tiled=True)
        else:
            pad = jnp.zeros((PAY_ROWS, time_dev), jnp.float32)
            pad = pad.at[0, : payload.shape[0]].set(payload)
            both = lax.all_gather(
                jnp.concatenate([grid_field, pad], axis=0), "sensor", axis=0, tiled=False
            )
            full_field = both[:, :sensor_dev, :].reshape(-1, time_dev)
            sensor_sum = jnp.sum(both[:, sensor_dev:, :], axis=0)
        left_product = jnp.dot(
            sensor_kernel, full_field, precision=PRECISE, preferred_element_type=jnp.float32
        )
        if payload is not None:
            left_product = jnp.concatenate([left_product, sensor_sum], axis=0)
        gathered = lax.all_gather(left_product, "tz", axis=1, tiled=True)
        gathered = lax.all_gather(gathered, ("tx", "ty"), axis=1, tiled=True)
        smooth = lax.dot_general(
            gathered[:sensor_dev],
            time_kernel,
            (((1,), (1,)), ((), ())),
            precision=PRECISE,
            preferred_element_type=jnp.float32,
        )
        field_rows = jnp.einsum(
            "bw,wij->bij", onehot, smooth.reshape(win_count, win_rows, time_dev), precision=PRECISE
        )
        interp_cols = jnp.einsum("bij,bjr->bir", field_rows, time_weights, precision=PRECISE)
        image = jnp.sum(sensor_weights * interp_cols, axis=1) + noise_var * vector
        if payload is None:
            return image, None
        totals = jnp.sum(
            gathered[sensor_dev:].reshape(PAY_ROWS, n_tm, time_dev), axis=1
        )[0, : payload.shape[0]]
        return image, totals

    residual0 = readings
    precond0 = inverse * residual0
    direction0 = precond0
    image0, _ = operator_apply(direction0)
    scaled_image0 = inverse * image0
    first_partials = jnp.stack(
        [jnp.sum(residual0 * precond0), jnp.sum(direction0 * image0)]
    )
    image_scaled, first_totals = operator_apply(scaled_image0, first_partials)
    inner0 = first_totals[0]
    step0 = inner0 / first_totals[1]
    solution = step0 * direction0
    residual1 = residual0 - step0 * image0
    precond1 = inverse * residual1
    image_precond1 = image0 - step0 * image_scaled
    second = butterfly_sum(
        jnp.stack(
            [
                jnp.sum(residual1 * precond1),
                jnp.sum(precond1 * image_precond1),
                jnp.sum(precond1 * image0 + direction0 * image_precond1),
            ]
        )
    )
    inner1 = second[0]
    ratio = inner1 / inner0
    direction1 = precond1 + ratio * direction0
    image1 = image_precond1 + ratio * image0
    curvature1 = second[1] + ratio * second[2] + ratio * ratio * first_totals[1]
    step1 = inner1 / curvature1
    solution = solution + step1 * direction1
    residual = residual1 - step1 * image1
    return (solution, residual)


def solution(mesh):
    n_sensor, n_tm = mesh.devices.shape
    devices = np.asarray(mesh.devices).reshape(n_sensor, n_tm // 8, 4, 2)
    mesh = Mesh(devices, ("sensor",) + TM)
    in_specs = (
        P(ALL, None),
        P(ALL, None),
        P(ALL, None, None),
        P(ALL, None, None),
        P(ALL),
        P("sensor", None),
        P(TM, None),
    )
    out_specs = (P(ALL, None), P(ALL, None))
    return jax.shard_map(
        on_device, mesh=mesh, in_specs=in_specs, out_specs=out_specs, check_vma=False
    )
```

```python
import jax
import jax.numpy as jnp
from jax import lax
import numpy as np
from jax.sharding import Mesh, PartitionSpec as P

PRECISE = lax.Precision.HIGH
PAY_ROWS = 8
TM = ("tx", "ty", "tz")
ALL = ("sensor",) + TM


def tm_index():
    return (
        lax.axis_index("tx") * (lax.axis_size("ty") * lax.axis_size("tz"))
        + lax.axis_index("ty") * lax.axis_size("tz")
        + lax.axis_index("tz")
    )


def butterfly_sum(value):
    for axis in ALL:
        size = lax.axis_size(axis)
        stride = 1
        while stride < size:
            value = value + lax.ppermute(value, axis, [(i, i ^ stride) for i in range(size)])
            stride *= 2
    return value


def on_device(
    readings, noise_var, sensor_weights, time_weights, window_index, sensor_kernel, time_kernel
):
    sensor_dev = sensor_kernel.shape[0]
    time_dev = time_kernel.shape[0]
    win_rows = sensor_weights.shape[1]
    win_count = sensor_dev // win_rows
    n_tm = time_kernel.shape[1] // time_dev
    window_ids = jnp.arange(win_count, dtype=jnp.int32)
    onehot = (window_index[:, None] == window_ids[None, :]).astype(jnp.float32)
    own_square = lax.dynamic_slice_in_dim(
        sensor_kernel, lax.axis_index("sensor") * sensor_dev, sensor_dev, 1
    )
    own_square = own_square.reshape(win_count, win_rows, win_count, win_rows)
    window_kernel = own_square[window_ids, :, window_ids, :]
    block_kernel = jnp.einsum("bw,wik->bik", onehot, window_kernel, precision=PRECISE)
    sensor_quad = jnp.sum(
        sensor_weights
        * jnp.einsum("bik,bkr->bir", block_kernel, sensor_weights, precision=PRECISE),
        axis=1,
    )
    time_square = lax.dynamic_slice_in_dim(
        time_kernel, tm_index() * time_dev, time_dev, 1
    )
    time_quad = jnp.sum(
        time_weights * jnp.einsum("jl,blr->bjr", time_square, time_weights, precision=PRECISE),
        axis=1,
    )
    inverse = 1.0 / (sensor_quad * time_quad + noise_var)

    def operator_apply(vector, payload=None):
        scaled = vector[:, None, :] * time_weights
        contrib = jnp.einsum("bir,bjr->bij", sensor_weights, scaled, precision=PRECISE)
        grid_field = jnp.einsum("bw,bij->wij", onehot, contrib, precision=PRECISE).reshape(
            sensor_dev, time_dev
        )
        if payload is None:
            full_field = lax.all_gather(grid_field, "sensor", axis=0, tiled=True)
        else:
            pad = jnp.zeros((PAY_ROWS, time_dev), jnp.float32)
            pad = pad.at[0, : payload.shape[0]].set(payload)
            both = lax.all_gather(
                jnp.concatenate([grid_field, pad], axis=0), "sensor", axis=0, tiled=False
            )
            full_field = both[:, :sensor_dev, :].reshape(-1, time_dev)
            sensor_sum = jnp.sum(both[:, sensor_dev:, :], axis=0)
        left_product = jnp.dot(
            sensor_kernel, full_field, precision=PRECISE, preferred_element_type=jnp.float32
        )
        if payload is not None:
            left_product = jnp.concatenate([left_product, sensor_sum], axis=0)
        gathered = lax.all_gather(left_product, "tz", axis=1, tiled=True)
        gathered = lax.all_gather(gathered, ("tx", "ty"), axis=1, tiled=True)
        smooth = lax.dot_general(
            gathered[:sensor_dev],
            time_kernel,
            (((1,), (1,)), ((), ())),
            precision=PRECISE,
            preferred_element_type=jnp.float32,
        )
        field_rows = jnp.einsum(
            "bw,wij->bij", onehot, smooth.reshape(win_count, win_rows, time_dev), precision=PRECISE
        )
        interp_cols = jnp.einsum("bij,bjr->bir", field_rows, time_weights, precision=PRECISE)
        image = jnp.sum(sensor_weights * interp_cols, axis=1) + noise_var * vector
        if payload is None:
            return image, None
        totals = jnp.sum(
            gathered[sensor_dev:].reshape(PAY_ROWS, n_tm, time_dev), axis=1
        )[0, : payload.shape[0]]
        return image, totals

    residual0 = readings
    precond0 = inverse * residual0
    direction0 = precond0
    image0, _ = operator_apply(direction0)
    scaled_image0 = inverse * image0
    first_partials = jnp.stack(
        [jnp.sum(residual0 * precond0), jnp.sum(direction0 * image0)]
    )
    image_scaled, first_totals = operator_apply(scaled_image0, first_partials)
    inner0 = first_totals[0]
    step0 = inner0 / first_totals[1]
    solution = step0 * direction0
    residual1 = residual0 - step0 * image0
    precond1 = inverse * residual1
    image_precond1 = image0 - step0 * image_scaled
    second = butterfly_sum(
        jnp.stack(
            [
                jnp.sum(residual1 * precond1),
                jnp.sum(precond1 * image_precond1),
                jnp.sum(precond1 * image0 + direction0 * image_precond1),
            ]
        )
    )
    inner1 = second[0]
    ratio = inner1 / inner0
    direction1 = precond1 + ratio * direction0
    image1 = image_precond1 + ratio * image0
    curvature1 = second[1] + ratio * second[2] + ratio * ratio * first_totals[1]
    step1 = inner1 / curvature1
    solution = solution + step1 * direction1
    residual = residual1 - step1 * image1
    return (solution, residual)


def solution(mesh):
    n_sensor, n_tm = mesh.devices.shape
    devices = np.asarray(mesh.devices).reshape(n_sensor, n_tm // 8, 4, 2)
    mesh = Mesh(devices, ("sensor",) + TM)
    in_specs = (
        P(ALL, None),
        P(ALL, None),
        P(ALL, None, None),
        P(ALL, None, None),
        P(ALL),
        P("sensor", None),
        P(TM, None),
    )
    out_specs = (P(ALL, None), P(ALL, None))
    return jax.shard_map(
        on_device, mesh=mesh, in_specs=in_specs, out_specs=out_specs, check_vma=False
    )
```

```python
import jax
import jax.numpy as jnp
from jax import lax
import numpy as np
from jax.sharding import Mesh, PartitionSpec as P

PRECISE = lax.Precision.HIGHEST
PAY_ROWS = 8
TM = ("tx", "ty", "tz")
ALL = ("sensor",) + TM


def tm_index():
    return (
        lax.axis_index("tx") * (lax.axis_size("ty") * lax.axis_size("tz"))
        + lax.axis_index("ty") * lax.axis_size("tz")
        + lax.axis_index("tz")
    )


def all_device_sum(value):
    count = 1
    for axis in ALL:
        count *= lax.axis_size(axis)
    copies = jnp.broadcast_to(value[None, :], (count, value.shape[0]))
    rows = lax.all_to_all(copies, ALL, 0, 0, tiled=True)
    return jnp.sum(rows, axis=0)


def on_device(
    readings, noise_var, sensor_weights, time_weights, window_index, sensor_kernel, time_kernel
):
    sensor_dev = sensor_kernel.shape[0]
    time_dev = time_kernel.shape[0]
    win_rows = sensor_weights.shape[1]
    win_count = sensor_dev // win_rows
    n_tm = time_kernel.shape[1] // time_dev
    window_ids = jnp.arange(win_count, dtype=jnp.int32)
    onehot = (window_index[:, None] == window_ids[None, :]).astype(jnp.float32)
    own_square = lax.dynamic_slice_in_dim(
        sensor_kernel, lax.axis_index("sensor") * sensor_dev, sensor_dev, 1
    )
    own_square = own_square.reshape(win_count, win_rows, win_count, win_rows)
    window_kernel = own_square[window_ids, :, window_ids, :]
    block_kernel = jnp.einsum("bw,wik->bik", onehot, window_kernel, precision=PRECISE)
    sensor_quad = jnp.sum(
        sensor_weights
        * jnp.einsum("bik,bkr->bir", block_kernel, sensor_weights, precision=PRECISE),
        axis=1,
    )
    time_square = lax.dynamic_slice_in_dim(
        time_kernel, tm_index() * time_dev, time_dev, 1
    )
    time_quad = jnp.sum(
        time_weights * jnp.einsum("jl,blr->bjr", time_square, time_weights, precision=PRECISE),
        axis=1,
    )
    inverse = 1.0 / (sensor_quad * time_quad + noise_var)

    def operator_apply(vector, payload=None):
        scaled = vector[:, None, :] * time_weights
        contrib = jnp.einsum("bir,bjr->bij", sensor_weights, scaled, precision=PRECISE)
        grid_field = jnp.einsum("bw,bij->wij", onehot, contrib, precision=PRECISE).reshape(
            sensor_dev, time_dev
        )
        if payload is None:
            full_field = lax.all_gather(grid_field, "sensor", axis=0, tiled=True)
        else:
            pad = jnp.zeros((PAY_ROWS, time_dev), jnp.float32)
            pad = pad.at[0, : payload.shape[0]].set(payload)
            both = lax.all_gather(
                jnp.concatenate([grid_field, pad], axis=0), "sensor", axis=0, tiled=False
            )
            full_field = both[:, :sensor_dev, :].reshape(-1, time_dev)
            sensor_sum = jnp.sum(both[:, sensor_dev:, :], axis=0)
        left_product = jnp.dot(
            sensor_kernel, full_field, precision=PRECISE, preferred_element_type=jnp.float32
        )
        if payload is not None:
            left_product = jnp.concatenate([left_product, sensor_sum], axis=0)
        gathered = lax.all_gather(left_product, "tz", axis=1, tiled=True)
        gathered = lax.all_gather(gathered, ("tx", "ty"), axis=1, tiled=True)
        smooth = lax.dot_general(
            gathered[:sensor_dev],
            time_kernel,
            (((1,), (1,)), ((), ())),
            precision=PRECISE,
            preferred_element_type=jnp.float32,
        )
        field_rows = jnp.einsum(
            "bw,wij->bij", onehot, smooth.reshape(win_count, win_rows, time_dev), precision=PRECISE
        )
        interp_cols = jnp.einsum("bij,bjr->bir", field_rows, time_weights, precision=PRECISE)
        image = jnp.sum(sensor_weights * interp_cols, axis=1) + noise_var * vector
        if payload is None:
            return image, None
        totals = jnp.sum(
            gathered[sensor_dev:].reshape(PAY_ROWS, n_tm, time_dev), axis=1
        )[0, : payload.shape[0]]
        return image, totals

    residual0 = readings
    precond0 = inverse * residual0
    direction0 = precond0
    image0, _ = operator_apply(direction0)
    scaled_image0 = inverse * image0
    first_partials = jnp.stack(
        [jnp.sum(residual0 * precond0), jnp.sum(direction0 * image0)]
    )
    image_scaled, first_totals = operator_apply(scaled_image0, first_partials)
    inner0 = first_totals[0]
    step0 = inner0 / first_totals[1]
    solution = step0 * direction0
    residual1 = residual0 - step0 * image0
    precond1 = inverse * residual1
    image_precond1 = image0 - step0 * image_scaled
    second = all_device_sum(
        jnp.stack(
            [
                jnp.sum(residual1 * precond1),
                jnp.sum(precond1 * image_precond1),
                jnp.sum(precond1 * image0 + direction0 * image_precond1),
            ]
        )
    )
    inner1 = second[0]
    ratio = inner1 / inner0
    direction1 = precond1 + ratio * direction0
    image1 = image_precond1 + ratio * image0
    curvature1 = second[1] + ratio * second[2] + ratio * ratio * first_totals[1]
    step1 = inner1 / curvature1
    solution = solution + step1 * direction1
    residual = residual1 - step1 * image1
    return (solution, residual)


def solution(mesh):
    n_sensor, n_tm = mesh.devices.shape
    devices = np.asarray(mesh.devices).reshape(n_sensor, n_tm // 8, 4, 2)
    mesh = Mesh(devices, ("sensor",) + TM)
    in_specs = (
        P(ALL, None),
        P(ALL, None),
        P(ALL, None, None),
        P(ALL, None, None),
        P(ALL),
        P("sensor", None),
        P(TM, None),
    )
    out_specs = (P(ALL, None), P(ALL, None))
    return jax.shard_map(
        on_device, mesh=mesh, in_specs=in_specs, out_specs=out_specs, check_vma=False
    )
```

```python
import jax
import jax.numpy as jnp
from jax import lax
import numpy as np
from jax.sharding import Mesh, PartitionSpec as P

PRECISE = lax.Precision.HIGHEST
PAY_ROWS = 8
TM = ("tx", "ty", "tz")
ALL = ("sensor",) + TM


def tm_index():
    return (
        lax.axis_index("tx") * (lax.axis_size("ty") * lax.axis_size("tz"))
        + lax.axis_index("ty") * lax.axis_size("tz")
        + lax.axis_index("tz")
    )


def all_device_sum(value):
    count = 1
    for axis in ALL:
        count *= lax.axis_size(axis)
    copies = jnp.broadcast_to(value[None, :], (count, value.shape[0]))
    rows = lax.all_to_all(copies, ALL, 0, 0, tiled=True)
    return jnp.sum(rows, axis=0)


def on_device(
    readings, noise_var, sensor_weights, time_weights, window_index, sensor_kernel, time_kernel
):
    sensor_dev = sensor_kernel.shape[0]
    time_dev = time_kernel.shape[0]
    win_rows = sensor_weights.shape[1]
    win_count = sensor_dev // win_rows
    n_tm = time_kernel.shape[1] // time_dev
    window_ids = jnp.arange(win_count, dtype=jnp.int32)
    onehot = (window_index[:, None] == window_ids[None, :]).astype(jnp.float32)
    own_square = lax.dynamic_slice_in_dim(
        sensor_kernel, lax.axis_index("sensor") * sensor_dev, sensor_dev, 1
    )
    own_square = own_square.reshape(win_count, win_rows, win_count, win_rows)
    window_kernel = own_square[window_ids, :, window_ids, :]
    block_kernel = jnp.einsum("bw,wik->bik", onehot, window_kernel, precision=PRECISE)
    sensor_quad = jnp.sum(
        sensor_weights
        * jnp.einsum("bik,bkr->bir", block_kernel, sensor_weights, precision=PRECISE),
        axis=1,
    )
    time_square = lax.dynamic_slice_in_dim(
        time_kernel, tm_index() * time_dev, time_dev, 1
    )
    time_quad = jnp.sum(
        time_weights * jnp.einsum("jl,blr->bjr", time_square, time_weights, precision=PRECISE),
        axis=1,
    )
    inverse = 1.0 / (sensor_quad * time_quad + noise_var)

    def operator_apply(vector, payload=None):
        scaled = vector[:, None, :] * time_weights
        contrib = jnp.einsum("bir,bjr->bij", sensor_weights, scaled, precision=PRECISE)
        grid_field = jnp.einsum("bw,bij->wij", onehot, contrib, precision=PRECISE).reshape(
            sensor_dev, time_dev
        )
        if payload is None:
            full_field = lax.all_gather(grid_field, "sensor", axis=0, tiled=True)
        else:
            pad = jnp.zeros((PAY_ROWS, time_dev), jnp.float32)
            pad = pad.at[0, : payload.shape[0]].set(payload)
            full_field, pads = lax.all_gather((grid_field, pad), "sensor", axis=0, tiled=True)
            pad = jnp.sum(pads.reshape(-1, PAY_ROWS, time_dev), axis=0)
        left_product = jnp.dot(
            sensor_kernel, full_field, precision=PRECISE, preferred_element_type=jnp.float32
        )
        if payload is None:
            gathered = lax.all_gather(left_product, "tz", axis=1, tiled=True)
            gathered = lax.all_gather(gathered, ("tx", "ty"), axis=1, tiled=True)
        else:
            gathered, pad = lax.all_gather((left_product, pad), "tz", axis=1, tiled=True)
            gathered, pad = lax.all_gather((gathered, pad), ("tx", "ty"), axis=1, tiled=True)
        smooth = lax.dot_general(
            gathered,
            time_kernel,
            (((1,), (1,)), ((), ())),
            precision=PRECISE,
            preferred_element_type=jnp.float32,
        )
        field_rows = jnp.einsum(
            "bw,wij->bij", onehot, smooth.reshape(win_count, win_rows, time_dev), precision=PRECISE
        )
        interp_cols = jnp.einsum("bij,bjr->bir", field_rows, time_weights, precision=PRECISE)
        image = jnp.sum(sensor_weights * interp_cols, axis=1) + noise_var * vector
        if payload is None:
            return image, None
        totals = jnp.sum(pad.reshape(PAY_ROWS, n_tm, time_dev), axis=1)[0, : payload.shape[0]]
        return image, totals

    residual0 = readings
    precond0 = inverse * residual0
    direction0 = precond0
    image0, _ = operator_apply(direction0)
    scaled_image0 = inverse * image0
    first_partials = jnp.stack(
        [jnp.sum(residual0 * precond0), jnp.sum(direction0 * image0)]
    )
    image_scaled, first_totals = operator_apply(scaled_image0, first_partials)
    inner0 = first_totals[0]
    step0 = inner0 / first_totals[1]
    solution = step0 * direction0
    residual1 = residual0 - step0 * image0
    precond1 = inverse * residual1
    image_precond1 = image0 - step0 * image_scaled
    second = all_device_sum(
        jnp.stack(
            [
                jnp.sum(residual1 * precond1),
                jnp.sum(precond1 * image_precond1),
                jnp.sum(precond1 * image0 + direction0 * image_precond1),
            ]
        )
    )
    inner1 = second[0]
    ratio = inner1 / inner0
    direction1 = precond1 + ratio * direction0
    image1 = image_precond1 + ratio * image0
    curvature1 = second[1] + ratio * second[2] + ratio * ratio * first_totals[1]
    step1 = inner1 / curvature1
    solution = solution + step1 * direction1
    residual = residual1 - step1 * image1
    return (solution, residual)


def solution(mesh):
    n_sensor, n_tm = mesh.devices.shape
    devices = np.asarray(mesh.devices).reshape(n_sensor, n_tm // 8, 4, 2)
    mesh = Mesh(devices, ("sensor",) + TM)
    in_specs = (
        P(ALL, None),
        P(ALL, None),
        P(ALL, None, None),
        P(ALL, None, None),
        P(ALL),
        P("sensor", None),
        P(TM, None),
    )
    out_specs = (P(ALL, None), P(ALL, None))
    return jax.shard_map(
        on_device, mesh=mesh, in_specs=in_specs, out_specs=out_specs, check_vma=False
    )
```

```python
import jax
import jax.numpy as jnp
from jax import lax
import numpy as np
from jax.sharding import Mesh, PartitionSpec as P

PRECISE = lax.Precision.HIGHEST
PAY_ROWS = 8
TM = ("tx", "ty", "tz")
ALL = ("sensor",) + TM


def tm_index():
    return (
        lax.axis_index("tx") * (lax.axis_size("ty") * lax.axis_size("tz"))
        + lax.axis_index("ty") * lax.axis_size("tz")
        + lax.axis_index("tz")
    )


def all_device_sum(value):
    count = 1
    for axis in ALL:
        count *= lax.axis_size(axis)
    copies = jnp.broadcast_to(value[None, :], (count, value.shape[0]))
    rows = lax.all_to_all(copies, ALL, 0, 0, tiled=True)
    return jnp.sum(rows, axis=0)


def on_device(
    readings, noise_var, sensor_weights, time_weights, window_index, sensor_kernel, time_kernel
):
    sensor_dev = sensor_kernel.shape[0]
    time_dev = time_kernel.shape[0]
    win_rows = sensor_weights.shape[1]
    win_count = sensor_dev // win_rows
    n_tm = time_kernel.shape[1] // time_dev
    window_ids = jnp.arange(win_count, dtype=jnp.int32)
    onehot = (window_index[:, None] == window_ids[None, :]).astype(jnp.float32)
    first_col = lax.axis_index("sensor") * sensor_dev
    window_kernel = jnp.stack(
        [
            lax.dynamic_slice(
                sensor_kernel, (w * win_rows, first_col + w * win_rows), (win_rows, win_rows)
            )
            for w in range(win_count)
        ]
    )
    block_kernel = jnp.einsum("bw,wik->bik", onehot, window_kernel, precision=PRECISE)
    sensor_quad = jnp.sum(
        sensor_weights
        * jnp.einsum("bik,bkr->bir", block_kernel, sensor_weights, precision=PRECISE),
        axis=1,
    )
    time_square = lax.dynamic_slice_in_dim(
        time_kernel, tm_index() * time_dev, time_dev, 1
    )
    time_quad = jnp.sum(
        time_weights * jnp.einsum("jl,blr->bjr", time_square, time_weights, precision=PRECISE),
        axis=1,
    )
    inverse = 1.0 / (sensor_quad * time_quad + noise_var)

    def operator_apply(vector, payload=None):
        scaled = vector[:, None, :] * time_weights
        contrib = jnp.einsum("bir,bjr->bij", sensor_weights, scaled, precision=PRECISE)
        grid_field = jnp.einsum("bw,bij->wij", onehot, contrib, precision=PRECISE).reshape(
            sensor_dev, time_dev
        )
        if payload is None:
            full_field = lax.all_gather(grid_field, "sensor", axis=0, tiled=True)
        else:
            pad = jnp.zeros((PAY_ROWS, time_dev), jnp.float32)
            pad = pad.at[0, : payload.shape[0]].set(payload)
            full_field, pads = lax.all_gather((grid_field, pad), "sensor", axis=0, tiled=True)
            pad = jnp.sum(pads.reshape(-1, PAY_ROWS, time_dev), axis=0)
        left_product = jnp.dot(
            sensor_kernel, full_field, precision=PRECISE, preferred_element_type=jnp.float32
        )
        if payload is None:
            gathered = lax.all_gather(left_product, "tz", axis=1, tiled=True)
            gathered = lax.all_gather(gathered, ("tx", "ty"), axis=1, tiled=True)
        else:
            gathered, pad = lax.all_gather((left_product, pad), "tz", axis=1, tiled=True)
            gathered, pad = lax.all_gather((gathered, pad), ("tx", "ty"), axis=1, tiled=True)
        smooth = lax.dot_general(
            gathered,
            time_kernel,
            (((1,), (1,)), ((), ())),
            precision=PRECISE,
            preferred_element_type=jnp.float32,
        )
        field_rows = jnp.einsum(
            "bw,wij->bij", onehot, smooth.reshape(win_count, win_rows, time_dev), precision=PRECISE
        )
        interp_cols = jnp.einsum("bij,bjr->bir", field_rows, time_weights, precision=PRECISE)
        image = jnp.sum(sensor_weights * interp_cols, axis=1) + noise_var * vector
        if payload is None:
            return image, None
        totals = jnp.sum(pad.reshape(PAY_ROWS, n_tm, time_dev), axis=1)[0, : payload.shape[0]]
        return image, totals

    residual0 = readings
    precond0 = inverse * residual0
    direction0 = precond0
    image0, _ = operator_apply(direction0)
    scaled_image0 = inverse * image0
    first_partials = jnp.stack(
        [jnp.sum(residual0 * precond0), jnp.sum(direction0 * image0)]
    )
    image_scaled, first_totals = operator_apply(scaled_image0, first_partials)
    inner0 = first_totals[0]
    step0 = inner0 / first_totals[1]
    solution = step0 * direction0
    residual1 = residual0 - step0 * image0
    precond1 = inverse * residual1
    image_precond1 = image0 - step0 * image_scaled
    second = all_device_sum(
        jnp.stack(
            [
                jnp.sum(residual1 * precond1),
                jnp.sum(precond1 * image_precond1),
                jnp.sum(precond1 * image0 + direction0 * image_precond1),
            ]
        )
    )
    inner1 = second[0]
    ratio = inner1 / inner0
    direction1 = precond1 + ratio * direction0
    image1 = image_precond1 + ratio * image0
    curvature1 = second[1] + ratio * second[2] + ratio * ratio * first_totals[1]
    step1 = inner1 / curvature1
    solution = solution + step1 * direction1
    residual = residual1 - step1 * image1
    return (solution, residual)


def solution(mesh):
    n_sensor, n_tm = mesh.devices.shape
    devices = np.asarray(mesh.devices).reshape(n_sensor, n_tm // 8, 4, 2)
    mesh = Mesh(devices, ("sensor",) + TM)
    in_specs = (
        P(ALL, None),
        P(ALL, None),
        P(ALL, None, None),
        P(ALL, None, None),
        P(ALL),
        P("sensor", None),
        P(TM, None),
    )
    out_specs = (P(ALL, None), P(ALL, None))
    return jax.shard_map(
        on_device, mesh=mesh, in_specs=in_specs, out_specs=out_specs, check_vma=False
    )
```

```python
import jax
import jax.numpy as jnp
from jax import lax
import numpy as np
from jax.sharding import Mesh, PartitionSpec as P

PRECISE = lax.Precision.HIGHEST
PAY_ROWS = 8
TM = ("tx", "ty", "tz")
ALL = ("sensor",) + TM


def tm_index():
    return (
        lax.axis_index("tx") * (lax.axis_size("ty") * lax.axis_size("tz"))
        + lax.axis_index("ty") * lax.axis_size("tz")
        + lax.axis_index("tz")
    )


def all_device_sum(value):
    count = 1
    for axis in ALL:
        count *= lax.axis_size(axis)
    copies = jnp.broadcast_to(value[None, :], (count, value.shape[0]))
    rows = lax.all_to_all(copies, ALL, 0, 0, tiled=True)
    return jnp.sum(rows, axis=0)


def on_device(
    readings, noise_var, sensor_weights, time_weights, window_index, sensor_kernel, time_kernel
):
    sensor_dev = sensor_kernel.shape[0]
    time_dev = time_kernel.shape[0]
    win_rows = sensor_weights.shape[1]
    win_count = sensor_dev // win_rows
    n_tm = time_kernel.shape[1] // time_dev
    window_ids = jnp.arange(win_count, dtype=jnp.int32)
    onehot = (window_index[:, None] == window_ids[None, :]).astype(jnp.float32)
    first_col = lax.axis_index("sensor") * sensor_dev
    window_kernel = jnp.stack(
        [
            lax.dynamic_slice(
                sensor_kernel, (w * win_rows, first_col + w * win_rows), (win_rows, win_rows)
            )
            for w in range(win_count)
        ]
    )
    block_kernel = jnp.einsum("bw,wik->bik", onehot, window_kernel, precision=PRECISE)
    sensor_quad = jnp.sum(
        sensor_weights
        * jnp.einsum("bik,bkr->bir", block_kernel, sensor_weights, precision=PRECISE),
        axis=1,
    )
    time_square = lax.dynamic_slice_in_dim(
        time_kernel, tm_index() * time_dev, time_dev, 1
    )
    time_quad = jnp.sum(
        time_weights * jnp.einsum("jl,blr->bjr", time_square, time_weights, precision=PRECISE),
        axis=1,
    )
    inverse = 1.0 / (sensor_quad * time_quad + noise_var)

    def operator_apply(vector, payload=None):
        scaled = vector[:, None, :] * time_weights
        contrib = jnp.einsum("bir,bjr->bij", sensor_weights, scaled, precision=PRECISE)
        grid_field = jnp.einsum("bw,bij->wij", onehot, contrib, precision=PRECISE).reshape(
            sensor_dev, time_dev
        )
        if payload is None:
            full_field = lax.all_gather(grid_field, "sensor", axis=0, tiled=True)
        else:
            pad = jnp.zeros((PAY_ROWS, time_dev), jnp.float32)
            pad = pad.at[0, : payload.shape[0]].set(payload)
            full_field, pads = lax.all_gather((grid_field, pad), "sensor", axis=0, tiled=True)
            pad = jnp.sum(pads.reshape(-1, PAY_ROWS, time_dev), axis=0)
        half = sensor_dev // 2
        swap = [(0, 1), (1, 0)]
        own_parts, other_parts = [], []
        for rows in (slice(0, half), slice(half, sensor_dev)):
            part = jnp.dot(
                sensor_kernel[rows], full_field, precision=PRECISE,
                preferred_element_type=jnp.float32,
            )
            own_parts.append(part)
            other_parts.append(lax.ppermute(part, "tz", swap))
        own = jnp.concatenate(own_parts, axis=0)
        other = jnp.concatenate(other_parts, axis=0)
        gathered = jnp.where(
            lax.axis_index("tz") == 0,
            jnp.concatenate([own, other], axis=1),
            jnp.concatenate([other, own], axis=1),
        )
        if payload is None:
            gathered = lax.all_gather(gathered, ("tx", "ty"), axis=1, tiled=True)
        else:
            pad = lax.all_gather(pad, "tz", axis=1, tiled=True)
            gathered, pad = lax.all_gather((gathered, pad), ("tx", "ty"), axis=1, tiled=True)
        smooth = lax.dot_general(
            gathered,
            time_kernel,
            (((1,), (1,)), ((), ())),
            precision=PRECISE,
            preferred_element_type=jnp.float32,
        )
        field_rows = jnp.einsum(
            "bw,wij->bij", onehot, smooth.reshape(win_count, win_rows, time_dev), precision=PRECISE
        )
        interp_cols = jnp.einsum("bij,bjr->bir", field_rows, time_weights, precision=PRECISE)
        image = jnp.sum(sensor_weights * interp_cols, axis=1) + noise_var * vector
        if payload is None:
            return image, None
        totals = jnp.sum(pad.reshape(PAY_ROWS, n_tm, time_dev), axis=1)[0, : payload.shape[0]]
        return image, totals

    residual0 = readings
    precond0 = inverse * residual0
    direction0 = precond0
    image0, _ = operator_apply(direction0)
    scaled_image0 = inverse * image0
    first_partials = jnp.stack(
        [jnp.sum(residual0 * precond0), jnp.sum(direction0 * image0)]
    )
    image_scaled, first_totals = operator_apply(scaled_image0, first_partials)
    inner0 = first_totals[0]
    step0 = inner0 / first_totals[1]
    solution = step0 * direction0
    residual1 = residual0 - step0 * image0
    precond1 = inverse * residual1
    image_precond1 = image0 - step0 * image_scaled
    second = all_device_sum(
        jnp.stack(
            [
                jnp.sum(residual1 * precond1),
                jnp.sum(precond1 * image_precond1),
                jnp.sum(precond1 * image0 + direction0 * image_precond1),
            ]
        )
    )
    inner1 = second[0]
    ratio = inner1 / inner0
    direction1 = precond1 + ratio * direction0
    image1 = image_precond1 + ratio * image0
    curvature1 = second[1] + ratio * second[2] + ratio * ratio * first_totals[1]
    step1 = inner1 / curvature1
    solution = solution + step1 * direction1
    residual = residual1 - step1 * image1
    return (solution, residual)


def solution(mesh):
    n_sensor, n_tm = mesh.devices.shape
    devices = np.asarray(mesh.devices).reshape(n_sensor, n_tm // 8, 4, 2)
    mesh = Mesh(devices, ("sensor",) + TM)
    in_specs = (
        P(ALL, None),
        P(ALL, None),
        P(ALL, None, None),
        P(ALL, None, None),
        P(ALL),
        P("sensor", None),
        P(TM, None),
    )
    out_specs = (P(ALL, None), P(ALL, None))
    return jax.shard_map(
        on_device, mesh=mesh, in_specs=in_specs, out_specs=out_specs, check_vma=False
    )
```

```python
import jax
import jax.numpy as jnp
from jax import lax
import numpy as np
from jax.sharding import Mesh, PartitionSpec as P

PRECISE = lax.Precision.HIGHEST
PAY_ROWS = 8
TM = ("tx", "ty", "tz")
ALL = ("sensor",) + TM
Z_SWAP = [(0, 1), (1, 0)]


def tm_index():
    return (
        lax.axis_index("tx") * (lax.axis_size("ty") * lax.axis_size("tz"))
        + lax.axis_index("ty") * lax.axis_size("tz")
        + lax.axis_index("tz")
    )


def all_device_sum(value):
    count = 1
    for axis in ALL:
        count *= lax.axis_size(axis)
    copies = jnp.broadcast_to(value[None, :], (count, value.shape[0]))
    rows = lax.all_to_all(copies, ALL, 0, 0, tiled=True)
    return jnp.sum(rows, axis=0)


def on_device(
    readings, noise_var, sensor_weights, time_weights, window_index, sensor_kernel, time_kernel
):
    sensor_dev = sensor_kernel.shape[0]
    time_dev = time_kernel.shape[0]
    win_rows = sensor_weights.shape[1]
    win_count = sensor_dev // win_rows
    n_tm = time_kernel.shape[1] // time_dev
    window_ids = jnp.arange(win_count, dtype=jnp.int32)
    onehot = (window_index[:, None] == window_ids[None, :]).astype(jnp.float32)
    first_col = lax.axis_index("sensor") * sensor_dev
    window_kernel = jnp.stack(
        [
            lax.dynamic_slice(
                sensor_kernel, (w * win_rows, first_col + w * win_rows), (win_rows, win_rows)
            )
            for w in range(win_count)
        ]
    )
    block_kernel = jnp.einsum("bw,wik->bik", onehot, window_kernel, precision=PRECISE)
    sensor_quad = jnp.sum(
        sensor_weights
        * jnp.einsum("bik,bkr->bir", block_kernel, sensor_weights, precision=PRECISE),
        axis=1,
    )
    time_square = lax.dynamic_slice_in_dim(
        time_kernel, tm_index() * time_dev, time_dev, 1
    )
    time_quad = jnp.sum(
        time_weights * jnp.einsum("jl,blr->bjr", time_square, time_weights, precision=PRECISE),
        axis=1,
    )
    inverse = 1.0 / (sensor_quad * time_quad + noise_var)

    n_tx, n_ty, n_tz = lax.axis_size("tx"), lax.axis_size("ty"), lax.axis_size("tz")
    z_now = lax.axis_index("tz")
    by_half = time_kernel.reshape(time_dev, n_tx, n_ty, n_tz, time_dev)
    own_cols = lax.dynamic_index_in_dim(by_half, z_now, axis=3, keepdims=False)
    own_cols = own_cols.reshape(time_dev, -1)
    other_cols = lax.dynamic_index_in_dim(by_half, 1 - z_now, axis=3, keepdims=False)
    partner_cols = lax.ppermute(other_cols.reshape(time_dev, -1), "tz", Z_SWAP)

    def operator_apply(vector, payload=None):
        scaled = vector[:, None, :] * time_weights
        contrib = jnp.einsum("bir,bjr->bij", sensor_weights, scaled, precision=PRECISE)
        grid_field = jnp.einsum("bw,bij->wij", onehot, contrib, precision=PRECISE).reshape(
            sensor_dev, time_dev
        )
        if payload is None:
            full_field = lax.all_gather(grid_field, "sensor", axis=0, tiled=True)
        else:
            pad = jnp.zeros((PAY_ROWS, time_dev), jnp.float32)
            pad = pad.at[0, : payload.shape[0]].set(payload)
            full_field, pads = lax.all_gather((grid_field, pad), "sensor", axis=0, tiled=True)
            pad = jnp.sum(pads.reshape(-1, PAY_ROWS, time_dev), axis=0)
        left_product = jnp.dot(
            sensor_kernel, full_field, precision=PRECISE, preferred_element_type=jnp.float32
        )
        if payload is None:
            half_rows = lax.all_gather(left_product, ("tx", "ty"), axis=1, tiled=True)
        else:
            half_rows, pad = lax.all_gather((left_product, pad), ("tx", "ty"), axis=1, tiled=True)
            pad = jnp.sum(pad.reshape(PAY_ROWS, -1, time_dev), axis=1)
        for_partner = jnp.dot(
            half_rows, partner_cols.T, precision=PRECISE, preferred_element_type=jnp.float32
        )
        if payload is None:
            from_partner = lax.ppermute(for_partner, "tz", Z_SWAP)
        else:
            from_partner, pad_partner = lax.ppermute((for_partner, pad), "tz", Z_SWAP)
            pad = pad + pad_partner
        smooth = (
            jnp.dot(half_rows, own_cols.T, precision=PRECISE, preferred_element_type=jnp.float32)
            + from_partner
        )
        field_rows = jnp.einsum(
            "bw,wij->bij", onehot, smooth.reshape(win_count, win_rows, time_dev), precision=PRECISE
        )
        interp_cols = jnp.einsum("bij,bjr->bir", field_rows, time_weights, precision=PRECISE)
        image = jnp.sum(sensor_weights * interp_cols, axis=1) + noise_var * vector
        if payload is None:
            return image, None
        totals = pad[0, : payload.shape[0]]
        return image, totals

    residual0 = readings
    precond0 = inverse * residual0
    direction0 = precond0
    image0, _ = operator_apply(direction0)
    scaled_image0 = inverse * image0
    first_partials = jnp.stack(
        [jnp.sum(residual0 * precond0), jnp.sum(direction0 * image0)]
    )
    image_scaled, first_totals = operator_apply(scaled_image0, first_partials)
    inner0 = first_totals[0]
    step0 = inner0 / first_totals[1]
    solution = step0 * direction0
    residual1 = residual0 - step0 * image0
    precond1 = inverse * residual1
    image_precond1 = image0 - step0 * image_scaled
    second = all_device_sum(
        jnp.stack(
            [
                jnp.sum(residual1 * precond1),
                jnp.sum(precond1 * image_precond1),
                jnp.sum(precond1 * image0 + direction0 * image_precond1),
            ]
        )
    )
    inner1 = second[0]
    ratio = inner1 / inner0
    direction1 = precond1 + ratio * direction0
    image1 = image_precond1 + ratio * image0
    curvature1 = second[1] + ratio * second[2] + ratio * ratio * first_totals[1]
    step1 = inner1 / curvature1
    solution = solution + step1 * direction1
    residual = residual1 - step1 * image1
    return (solution, residual)


def solution(mesh):
    n_sensor, n_tm = mesh.devices.shape
    devices = np.asarray(mesh.devices).reshape(n_sensor, n_tm // 8, 4, 2)
    mesh = Mesh(devices, ("sensor",) + TM)
    in_specs = (
        P(ALL, None),
        P(ALL, None),
        P(ALL, None, None),
        P(ALL, None, None),
        P(ALL),
        P("sensor", None),
        P(TM, None),
    )
    out_specs = (P(ALL, None), P(ALL, None))
    return jax.shard_map(
        on_device, mesh=mesh, in_specs=in_specs, out_specs=out_specs, check_vma=False
    )
```

```python
import jax
import jax.numpy as jnp
from jax import lax
import numpy as np
from jax.sharding import Mesh, PartitionSpec as P

PRECISE = lax.Precision.HIGHEST
PAY_ROWS = 8
TM = ("tx", "ty", "tz")
ALL = ("sensor",) + TM
Z_SWAP = [(0, 1), (1, 0)]


def tm_index():
    return (
        lax.axis_index("tx") * (lax.axis_size("ty") * lax.axis_size("tz"))
        + lax.axis_index("ty") * lax.axis_size("tz")
        + lax.axis_index("tz")
    )


def all_device_sum(value):
    count = 1
    for axis in ALL:
        count *= lax.axis_size(axis)
    copies = jnp.broadcast_to(value[None, :], (count, value.shape[0]))
    rows = lax.all_to_all(copies, ALL, 0, 0, tiled=True)
    return jnp.sum(rows, axis=0)


def on_device(
    readings, noise_var, sensor_weights, time_weights, window_index, sensor_kernel, time_kernel
):
    sensor_dev = sensor_kernel.shape[0]
    time_dev = time_kernel.shape[0]
    win_rows = sensor_weights.shape[1]
    win_count = sensor_dev // win_rows
    n_tm = time_kernel.shape[1] // time_dev
    window_ids = jnp.arange(win_count, dtype=jnp.int32)
    onehot = (window_index[:, None] == window_ids[None, :]).astype(jnp.float32)
    first_col = lax.axis_index("sensor") * sensor_dev
    window_kernel = jnp.stack(
        [
            lax.dynamic_slice(
                sensor_kernel, (w * win_rows, first_col + w * win_rows), (win_rows, win_rows)
            )
            for w in range(win_count)
        ]
    )
    block_kernel = jnp.einsum("bw,wik->bik", onehot, window_kernel, precision=PRECISE)
    sensor_quad = jnp.sum(
        sensor_weights
        * jnp.einsum("bik,bkr->bir", block_kernel, sensor_weights, precision=PRECISE),
        axis=1,
    )
    time_square = lax.dynamic_slice_in_dim(
        time_kernel, tm_index() * time_dev, time_dev, 1
    )
    time_quad = jnp.sum(
        time_weights * jnp.einsum("jl,blr->bjr", time_square, time_weights, precision=PRECISE),
        axis=1,
    )
    inverse = 1.0 / (sensor_quad * time_quad + noise_var)

    n_tx, n_ty, n_tz = lax.axis_size("tx"), lax.axis_size("ty"), lax.axis_size("tz")
    z_now = lax.axis_index("tz")
    by_half = time_kernel.reshape(time_dev, n_tx, n_ty, n_tz, time_dev)
    half0 = by_half[:, :, :, 0, :].reshape(time_dev, -1)
    half1 = by_half[:, :, :, 1, :].reshape(time_dev, -1)
    own_cols = jnp.where(z_now == 0, half0, half1)
    other_cols = jnp.where(z_now == 0, half1, half0)
    other_cols, readings = lax.optimization_barrier((other_cols, readings))
    partner_cols = lax.ppermute(other_cols, "tz", Z_SWAP)

    def operator_apply(vector, payload=None):
        scaled = vector[:, None, :] * time_weights
        contrib = jnp.einsum("bir,bjr->bij", sensor_weights, scaled, precision=PRECISE)
        grid_field = jnp.einsum("bw,bij->wij", onehot, contrib, precision=PRECISE).reshape(
            sensor_dev, time_dev
        )
        kernel_cols = partner_cols
        if payload is None:
            full_field = lax.all_gather(grid_field, "sensor", axis=0, tiled=True)
            full_field, kernel_cols = lax.optimization_barrier((full_field, kernel_cols))
        else:
            pad = jnp.zeros((PAY_ROWS, time_dev), jnp.float32)
            pad = pad.at[0, : payload.shape[0]].set(payload)
            full_field, pads = lax.all_gather((grid_field, pad), "sensor", axis=0, tiled=True)
            pad = jnp.sum(pads.reshape(-1, PAY_ROWS, time_dev), axis=0)
        left_product = jnp.dot(
            sensor_kernel, full_field, precision=PRECISE, preferred_element_type=jnp.float32
        )
        if payload is None:
            half_rows = lax.all_gather(left_product, ("tx", "ty"), axis=1, tiled=True)
        else:
            half_rows, pad = lax.all_gather((left_product, pad), ("tx", "ty"), axis=1, tiled=True)
            pad = jnp.sum(pad.reshape(PAY_ROWS, -1, time_dev), axis=1)
        for_partner = jnp.dot(
            half_rows, kernel_cols.T, precision=PRECISE, preferred_element_type=jnp.float32
        )
        if payload is None:
            from_partner = lax.ppermute(for_partner, "tz", Z_SWAP)
        else:
            from_partner, pad_partner = lax.ppermute((for_partner, pad), "tz", Z_SWAP)
            pad = pad + pad_partner
        smooth = (
            jnp.dot(half_rows, own_cols.T, precision=PRECISE, preferred_element_type=jnp.float32)
            + from_partner
        )
        field_rows = jnp.einsum(
            "bw,wij->bij", onehot, smooth.reshape(win_count, win_rows, time_dev), precision=PRECISE
        )
        interp_cols = jnp.einsum("bij,bjr->bir", field_rows, time_weights, precision=PRECISE)
        image = jnp.sum(sensor_weights * interp_cols, axis=1) + noise_var * vector
        if payload is None:
            return image, None
        totals = pad[0, : payload.shape[0]]
        return image, totals

    residual0 = readings
    precond0 = inverse * residual0
    direction0 = precond0
    image0, _ = operator_apply(direction0)
    scaled_image0 = inverse * image0
    first_partials = jnp.stack(
        [jnp.sum(residual0 * precond0), jnp.sum(direction0 * image0)]
    )
    image_scaled, first_totals = operator_apply(scaled_image0, first_partials)
    inner0 = first_totals[0]
    step0 = inner0 / first_totals[1]
    solution = step0 * direction0
    residual1 = residual0 - step0 * image0
    precond1 = inverse * residual1
    image_precond1 = image0 - step0 * image_scaled
    second = all_device_sum(
        jnp.stack(
            [
                jnp.sum(residual1 * precond1),
                jnp.sum(precond1 * image_precond1),
                jnp.sum(precond1 * image0 + direction0 * image_precond1),
            ]
        )
    )
    inner1 = second[0]
    ratio = inner1 / inner0
    direction1 = precond1 + ratio * direction0
    image1 = image_precond1 + ratio * image0
    curvature1 = second[1] + ratio * second[2] + ratio * ratio * first_totals[1]
    step1 = inner1 / curvature1
    solution = solution + step1 * direction1
    residual = residual1 - step1 * image1
    return (solution, residual)


def solution(mesh):
    n_sensor, n_tm = mesh.devices.shape
    devices = np.asarray(mesh.devices).reshape(n_sensor, n_tm // 8, 4, 2)
    mesh = Mesh(devices, ("sensor",) + TM)
    in_specs = (
        P(ALL, None),
        P(ALL, None),
        P(ALL, None, None),
        P(ALL, None, None),
        P(ALL),
        P("sensor", None),
        P(TM, None),
    )
    out_specs = (P(ALL, None), P(ALL, None))
    return jax.shard_map(
        on_device, mesh=mesh, in_specs=in_specs, out_specs=out_specs, check_vma=False
    )
```

```python
import jax
import jax.numpy as jnp
from jax import lax
import numpy as np
from jax.sharding import Mesh, PartitionSpec as P

PRECISE = lax.Precision.HIGHEST
PAY_ROWS = 8
TM = ("tx", "ty", "tz")
ALL = ("sensor",) + TM
Z_SWAP = [(0, 1), (1, 0)]


def tm_index():
    return (
        lax.axis_index("tx") * (lax.axis_size("ty") * lax.axis_size("tz"))
        + lax.axis_index("ty") * lax.axis_size("tz")
        + lax.axis_index("tz")
    )


def all_device_sum(value):
    count = 1
    for axis in ALL:
        count *= lax.axis_size(axis)
    copies = jnp.broadcast_to(value[None, :], (count, value.shape[0]))
    rows = lax.all_to_all(copies, ALL, 0, 0, tiled=True)
    return jnp.sum(rows, axis=0)


def on_device(
    readings, noise_var, sensor_weights, time_weights, window_index, sensor_kernel, time_kernel
):
    sensor_dev = sensor_kernel.shape[0]
    time_dev = time_kernel.shape[0]
    win_rows = sensor_weights.shape[1]
    win_count = sensor_dev // win_rows
    n_tm = time_kernel.shape[1] // time_dev
    window_ids = jnp.arange(win_count, dtype=jnp.int32)
    onehot = (window_index[:, None] == window_ids[None, :]).astype(jnp.float32)
    first_col = lax.axis_index("sensor") * sensor_dev
    window_kernel = jnp.stack(
        [
            lax.dynamic_slice(
                sensor_kernel, (w * win_rows, first_col + w * win_rows), (win_rows, win_rows)
            )
            for w in range(win_count)
        ]
    )
    block_kernel = jnp.einsum("bw,wik->bik", onehot, window_kernel, precision=PRECISE)
    sensor_quad = jnp.sum(
        sensor_weights
        * jnp.einsum("bik,bkr->bir", block_kernel, sensor_weights, precision=PRECISE),
        axis=1,
    )
    time_square = lax.dynamic_slice_in_dim(
        time_kernel, tm_index() * time_dev, time_dev, 1
    )
    time_quad = jnp.sum(
        time_weights * jnp.einsum("jl,blr->bjr", time_square, time_weights, precision=PRECISE),
        axis=1,
    )
    inverse = 1.0 / (sensor_quad * time_quad + noise_var)

    n_tx, n_ty, n_tz = lax.axis_size("tx"), lax.axis_size("ty"), lax.axis_size("tz")
    z_now = lax.axis_index("tz")
    by_half = time_kernel.reshape(time_dev, n_tx, n_ty, n_tz, time_dev)
    half0 = by_half[:, :, :, 0, :].reshape(time_dev, -1)
    half1 = by_half[:, :, :, 1, :].reshape(time_dev, -1)
    own_cols = jnp.where(z_now == 0, half0, half1)
    other_cols = jnp.where(z_now == 0, half1, half0)
    partner_cols = lax.ppermute(other_cols, "tz", Z_SWAP)

    def operator_apply(vector, payload=None):
        scaled = vector[:, None, :] * time_weights
        contrib = jnp.einsum("bir,bjr->bij", sensor_weights, scaled, precision=PRECISE)
        grid_field = jnp.einsum("bw,bij->wij", onehot, contrib, precision=PRECISE).reshape(
            sensor_dev, time_dev
        )
        if payload is None:
            full_field = lax.all_gather(grid_field, "sensor", axis=0, tiled=True)
        else:
            pad = jnp.zeros((PAY_ROWS, time_dev), jnp.float32)
            pad = pad.at[0, : payload.shape[0]].set(payload)
            full_field, pads = lax.all_gather((grid_field, pad), "sensor", axis=0, tiled=True)
            pad = jnp.sum(pads.reshape(-1, PAY_ROWS, time_dev), axis=0)
        left_product = jnp.dot(
            sensor_kernel, full_field, precision=PRECISE, preferred_element_type=jnp.float32
        )
        if payload is None:
            half_rows = lax.all_gather(left_product, ("tx", "ty"), axis=1, tiled=True)
        else:
            half_rows, pad = lax.all_gather((left_product, pad), ("tx", "ty"), axis=1, tiled=True)
            pad = jnp.sum(pad.reshape(PAY_ROWS, -1, time_dev), axis=1)
        for_partner = jnp.dot(
            half_rows, partner_cols.T, precision=PRECISE, preferred_element_type=jnp.float32
        )
        if payload is None:
            from_partner = lax.ppermute(for_partner, "tz", Z_SWAP)
        else:
            from_partner, pad_partner = lax.ppermute((for_partner, pad), "tz", Z_SWAP)
            pad = pad + pad_partner
        smooth = (
            jnp.dot(half_rows, own_cols.T, precision=PRECISE, preferred_element_type=jnp.float32)
            + from_partner
        )
        field_rows = jnp.einsum(
            "bw,wij->bij", onehot, smooth.reshape(win_count, win_rows, time_dev), precision=PRECISE
        )
        interp_cols = jnp.einsum("bij,bjr->bir", field_rows, time_weights, precision=PRECISE)
        image = jnp.sum(sensor_weights * interp_cols, axis=1) + noise_var * vector
        if payload is None:
            return image, None
        totals = pad[0, : payload.shape[0]]
        return image, totals

    residual0 = readings
    precond0 = inverse * residual0
    direction0 = precond0
    image0, _ = operator_apply(direction0)
    scaled_image0 = inverse * image0
    first_partials = jnp.stack(
        [jnp.sum(residual0 * precond0), jnp.sum(direction0 * image0)]
    )
    image_scaled, first_totals = operator_apply(scaled_image0, first_partials)
    inner0 = first_totals[0]
    step0 = inner0 / first_totals[1]
    solution = step0 * direction0
    residual1 = residual0 - step0 * image0
    precond1 = inverse * residual1
    image_precond1 = image0 - step0 * image_scaled
    second = all_device_sum(
        jnp.stack(
            [
                jnp.sum(residual1 * precond1),
                jnp.sum(precond1 * image_precond1),
                jnp.sum(precond1 * image0 + direction0 * image_precond1),
            ]
        )
    )
    inner1 = second[0]
    ratio = inner1 / inner0
    direction1 = precond1 + ratio * direction0
    image1 = image_precond1 + ratio * image0
    curvature1 = second[1] + ratio * second[2] + ratio * ratio * first_totals[1]
    step1 = inner1 / curvature1
    solution = solution + step1 * direction1
    residual = residual1 - step1 * image1
    return (solution, residual)


def solution(mesh):
    n_sensor, n_tm = mesh.devices.shape
    devices = np.asarray(mesh.devices).reshape(n_sensor, n_tm // 8, 4, 2)
    mesh = Mesh(devices, ("sensor",) + TM)
    in_specs = (
        P(ALL, None),
        P(ALL, None),
        P(ALL, None, None),
        P(ALL, None, None),
        P(ALL),
        P("sensor", None),
        P(TM, None),
    )
    out_specs = (P(ALL, None), P(ALL, None))
    return jax.shard_map(
        on_device, mesh=mesh, in_specs=in_specs, out_specs=out_specs, check_vma=False
    )
```
